1024 devices in a mesh: segment: 16 (over z_hi, x), dp: 4 (over z_lo), tensor: 16 (over y, core).
Axes of the slice: x: 4, y: 8, z: 16 (z_hi: 4, z_lo: 4; z = z_hi * 4 + z_lo), core: 2. Of those that a mesh axis runs over, the one named last changes fastest.
Arguments:
- inbound: bfloat16 [16, 2, 512, 4096], P('segment', None, 'dp'), may hold values from -21 to 21
- weights: bfloat16 [16, 4096, 3, 4096], P('segment', None, None, 'tensor'), may hold values from -0.09375 to 0.09375
- cotangent: bfloat16 [16, 2, 512, 4096], P('segment', None, 'dp', 'tensor'), may hold values from -20 to 20
Outputs:
- section_out: bfloat16 [16, 2, 512, 4096], P('segment', None, 'dp', 'tensor')
The draws below stay inside these ranges and needn't reach their ends.
All inputs are finite; a program needn't handle non-finite values.
Results may differ from the reference program's by a relative error of at most 0.022.
The reference program's roundings to bfloat16 on the way count: a program that leaves them out, or rounds other values in their place, can miss the bound.
Values may be sent and summed in bfloat16 or wider, within the bound.
No kernel may reach another device: no remote copies, remote signals or barrier semaphores. Data moves between devices by JAX's collectives and lax.ppermute only.
A program may use at most 64 MiB of HBM per device.

```python
import math
import jax
import jax.numpy as jnp
from jax import lax

D = 4096
HD = 64
HEADS = 64
MB = 2
TOK = 512
N_SEGMENT = 16
N_TENSOR = 16


def draw_inbound(key, part):
    first_key, second_key = jax.random.split(key)
    base = jnp.clip(jax.random.normal(first_key, (N_SEGMENT, MB, TOK, D), jnp.float32), -6.0, 6.0)
    row_scale = jnp.exp(jax.random.uniform(second_key, (N_SEGMENT, MB, TOK, 1), jnp.float32, math.log(0.5), math.log(2.0)))
    return (base * row_scale).astype(jnp.bfloat16)


def draw_cotangent(key, part):
    slot_scale = jnp.where(jnp.arange(N_SEGMENT) == 0, 0.3, 4.0).astype(jnp.float32)[:, None, None, None]
    base = jnp.clip(jax.random.normal(key, (N_SEGMENT, MB, TOK, D), jnp.float32), -5.0, 5.0)
    return (base * slot_scale).astype(jnp.bfloat16)


def shard_levels(own_key, extent, cuts, least, high):
    level = 1.0
    for position, shards_of in cuts:
        draws = jax.random.uniform(jax.random.fold_in(jax.random.fold_in(own_key, 6), position), (shards_of,), jnp.float32, least / len(cuts), high / len(cuts))
        level = level * jnp.repeat(jnp.exp(draws), extent[position] // shards_of).reshape((-1,) + (1,) * (len(extent) - 1 - position))
    return level


def normal_values(key, dims, deviation, limit, cuts=(), kind=jnp.bfloat16):
    drawn = deviation * jax.random.normal(key, dims, jnp.float32)
    if cuts:
        drawn = drawn * shard_levels(key, dims, cuts, -0.22, 0.18)
    return jnp.clip(drawn, -limit, limit).astype(kind)


def setup_inputs(seed: int = 0) -> dict:
    keys = jax.random.split(jax.random.key(seed), 4)
    inbound = draw_inbound(jax.random.fold_in(keys[3], 71), 0)
    weights = normal_values(keys[1], (N_SEGMENT, D, 3, D), D ** -0.5, 0.09375, ((0, 16), (3, 16)))
    cotangent = draw_cotangent(jax.random.fold_in(keys[3], 71), 0)
    return {"inbound": inbound, "weights": weights, "cotangent": cotangent}


def one_section(section_states, encoder_states, section_weights, upstream):
    row_total = MB * TOK
    feat_width = D // N_TENSOR
    score_scale = HD ** -0.5
    query = jnp.dot(section_states.reshape(row_total, D), section_weights[:, 0, :], preferred_element_type=jnp.float32).astype(jnp.bfloat16)
    flat_enc = encoder_states.reshape(row_total, D)
    key_rows = jnp.dot(flat_enc, section_weights[:, 1, :], preferred_element_type=jnp.float32).astype(jnp.bfloat16)
    value_rows = jnp.dot(flat_enc, section_weights[:, 2, :], preferred_element_type=jnp.float32).astype(jnp.bfloat16)
    query_heads = query.reshape(MB, TOK, HEADS, HD).astype(jnp.float32)
    key_heads = key_rows.reshape(MB, TOK, HEADS, HD).astype(jnp.float32)
    value_heads = value_rows.reshape(MB, TOK, HEADS, HD).astype(jnp.float32)
    scores = jnp.einsum("mqhe,mkhe->mhqk", query_heads, key_heads) * score_scale
    score_peak = jnp.max(scores, axis=-1, keepdims=True)
    exp_scores = jnp.exp(scores - score_peak)
    attend_prob = exp_scores / jnp.sum(exp_scores, axis=-1, keepdims=True)
    prob_rounded = attend_prob.astype(jnp.bfloat16).astype(jnp.float32)
    context = jnp.einsum("mhqk,mkhe->mqhe", prob_rounded, value_heads).astype(jnp.bfloat16).reshape(MB, TOK, D)
    grad_heads = upstream.reshape(MB, TOK, HEADS, HD).astype(jnp.float32)
    prob_grad = jnp.einsum("mqhe,mkhe->mhqk", grad_heads, value_heads)
    row_delta = jnp.sum(attend_prob * prob_grad, axis=-1, keepdims=True)
    score_grad = (attend_prob * (prob_grad - row_delta) * score_scale).astype(jnp.bfloat16).astype(jnp.float32)
    key_grad = jnp.einsum("mhqk,mqhe->mkhe", score_grad, query_heads).astype(jnp.bfloat16)
    value_grad = jnp.einsum("mhqk,mqhe->mkhe", prob_rounded, grad_heads).astype(jnp.bfloat16)
    joined_grads = jnp.concatenate([key_grad.reshape(row_total, N_TENSOR, feat_width), value_grad.reshape(row_total, N_TENSOR, feat_width)], axis=2)
    joined_weights = jnp.concatenate([section_weights[:, 1, :].reshape(D, N_TENSOR, feat_width), section_weights[:, 2, :].reshape(D, N_TENSOR, feat_width)], axis=2)
    group_terms = jnp.einsum("rtc,dtc->trd", joined_grads.astype(jnp.float32), joined_weights.astype(jnp.float32))
    rounded_terms = lax.optimization_barrier(group_terms.astype(jnp.bfloat16)).astype(jnp.float32)
    section_grad = jnp.sum(rounded_terms, axis=0).reshape(MB, TOK, D)
    return context, section_grad


def reference(inbound, weights, cotangent):
    encoder_states = inbound[0]

    def run_section(index):
        return one_section(inbound[index], encoder_states, weights[index], cotangent[index])

    contexts, section_grads = lax.map(run_section, jnp.arange(1, N_SEGMENT, dtype=jnp.int32))
    encoder_grad = (cotangent[0].astype(jnp.float32) + jnp.sum(section_grads, axis=0)).astype(jnp.bfloat16)
    return jnp.concatenate([encoder_grad[None], contexts], axis=0)
```

```python
import jax
import jax.numpy as jnp
from jax import lax
from jax.sharding import PartitionSpec as P

HD = 64
X_SIZE = 4


def seg_tree(n_seg):
    n_hi = n_seg // X_SIZE
    rounds = []
    hi_round = [(0, X_SIZE)]
    if n_hi > 2:
        hi_round.append((0, (n_hi - 1) * X_SIZE))
    rounds.append(hi_round)
    if n_hi > 3:
        rounds.append([(X_SIZE, 2 * X_SIZE)])
    x_round = [(z * X_SIZE, z * X_SIZE + 1) for z in range(n_hi)]
    x_round2 = [(z * X_SIZE, z * X_SIZE + X_SIZE - 1) for z in range(n_hi)]
    rounds.append(x_round + x_round2)
    rounds.append([(z * X_SIZE + 1, z * X_SIZE + 2) for z in range(n_hi)])
    return rounds


def split_pairs(pairs):
    groups = []
    for pair in pairs:
        for group in groups:
            if all(pair[0] != p[0] and pair[1] != p[1] for p in group):
                group.append(pair)
                break
        else:
            groups.append([pair])
    return groups


def seg_broadcast(value, rounds):
    seg = lax.axis_index("segment")
    cur = value
    for pairs in rounds:
        nxt = cur
        for group in split_pairs(pairs):
            got = lax.ppermute(cur, "segment", group)
            dests = jnp.array([p[1] for p in group])
            nxt = jnp.where(jnp.any(seg == dests), got, nxt)
        cur = nxt
    return cur


def seg_reduce(value, rounds):
    seg = lax.axis_index("segment")
    cur = value
    for pairs in reversed(rounds):
        rev = [(b, a) for a, b in pairs]
        acc = cur
        for group in split_pairs(rev):
            got = lax.ppermute(cur, "segment", group)
            dests = jnp.array([p[1] for p in group])
            acc = acc + jnp.where(jnp.any(seg == dests), got, jnp.zeros_like(got))
        cur = acc
    return cur


def dp_gather_small(value, n_dp):
    parts = [value]
    for shift in range(1, n_dp):
        parts.append(lax.ppermute(value, "dp", [(i, (i + shift) % n_dp) for i in range(n_dp)]))
    return jnp.stack(parts)


def shards(inbound, weights, cotangent):
    n_seg = lax.axis_size("segment")
    n_dp = lax.axis_size("dp")
    n_tensor = lax.axis_size("tensor")
    seg = lax.axis_index("segment")
    tix = lax.axis_index("tensor")
    rounds = seg_tree(n_seg)

    states = inbound[0]
    micro_count, row_count, model_width = states.shape
    layer = weights[0]
    feat_width = layer.shape[2]
    head_count = feat_width // HD
    scale = HD ** (-0.5)
    rows = micro_count * row_count

    query = jnp.dot(
        states.reshape(rows, model_width), layer[:, 0, :], preferred_element_type=jnp.float32
    ).astype(jnp.bfloat16)
    query = query.reshape(micro_count, row_count, feat_width)
    upstream = cotangent[0]
    all_query = lax.all_gather(query, "dp", axis=1, tiled=True)
    all_grad = lax.all_gather(upstream, "dp", axis=1, tiled=True)
    query_count = all_query.shape[1]

    chunk = lax.dynamic_slice_in_dim(states, tix * (model_width // n_tensor), model_width // n_tensor, axis=2)
    chunk = seg_broadcast(chunk, rounds)
    encoded = lax.all_gather(chunk, "tensor", axis=2, tiled=True)

    pair_weights = layer[:, 1:, :].reshape(model_width, 2 * feat_width)
    keyval = jnp.dot(
        encoded.reshape(rows, model_width), pair_weights, preferred_element_type=jnp.float32
    ).astype(jnp.bfloat16)
    keyval = keyval.reshape(micro_count, row_count, 2, head_count, HD)
    key_heads = keyval[:, :, 0]
    value_heads = keyval[:, :, 1]
    query_heads = all_query.reshape(micro_count, query_count, head_count, HD)
    grad_heads = all_grad.reshape(micro_count, query_count, head_count, HD)

    scores = (
        jnp.einsum("mqhe,mkhe->mhqk", query_heads, key_heads, preferred_element_type=jnp.float32)
        * scale
    )
    prob_grad = jnp.einsum(
        "mqhe,mkhe->mhqk", grad_heads, value_heads, preferred_element_type=jnp.float32
    )
    local_peak = jnp.max(scores, axis=-1)
    local_exp = jnp.exp(scores - local_peak[..., None])
    local_sum = jnp.sum(local_exp, axis=-1)
    local_delta = jnp.sum(local_exp * prob_grad, axis=-1)
    stats = jnp.stack([local_peak, local_sum, local_delta])
    all_stats = dp_gather_small(stats, n_dp)
    peaks = all_stats[:, 0]
    peak = jnp.max(peaks, axis=0)
    weight = jnp.exp(peaks - peak[None])
    total = jnp.sum(all_stats[:, 1] * weight, axis=0)
    row_delta = jnp.sum(all_stats[:, 2] * weight, axis=0) / total

    attend_prob = jnp.exp(scores - peak[..., None]) / total[..., None]
    prob_rounded = attend_prob.astype(jnp.bfloat16)
    score_grad = (attend_prob * (prob_grad - row_delta[..., None]) * scale).astype(jnp.bfloat16)

    context_part = jnp.einsum(
        "mhqk,mkhe->mqhe", prob_rounded, value_heads, preferred_element_type=jnp.float32
    ).reshape(micro_count, query_count, feat_width)
    context = lax.psum_scatter(context_part, "dp", scatter_dimension=1, tiled=True).astype(
        jnp.bfloat16
    )

    key_grad = jnp.einsum(
        "mhqk,mqhe->mkhe", score_grad, query_heads, preferred_element_type=jnp.float32
    ).astype(jnp.bfloat16)
    value_grad = jnp.einsum(
        "mhqk,mqhe->mkhe", prob_rounded, grad_heads, preferred_element_type=jnp.float32
    ).astype(jnp.bfloat16)
    joined = jnp.stack(
        [key_grad.reshape(rows, feat_width), value_grad.reshape(rows, feat_width)], axis=1
    ).reshape(rows, 2 * feat_width)
    head_terms = jnp.einsum(
        "rc,dc->rd", joined, pair_weights, preferred_element_type=jnp.float32
    ).astype(jnp.bfloat16)
    head_terms = head_terms.reshape(micro_count, row_count, model_width)
    heads_total = lax.psum_scatter(head_terms, "tensor", scatter_dimension=2, tiled=True).astype(
        jnp.float32
    )
    heads_total = jnp.where(seg > 0, heads_total, jnp.zeros_like(heads_total))
    sections = seg_reduce(heads_total, rounds)
    encoder_grad = (sections + cotangent[0].astype(jnp.float32)).astype(jnp.bfloat16)
    result = jnp.where(seg == 0, encoder_grad, context)
    return result[None]


def solution(mesh):
    placed = (
        P("segment", None, "dp", None),
        P("segment", None, None, "tensor"),
        P("segment", None, "dp", "tensor"),
    )
    return jax.shard_map(
        shards,
        mesh=mesh,
        in_specs=placed,
        out_specs=P("segment", None, "dp", "tensor"),
        check_vma=False,
    )
```

```python
import jax
import jax.numpy as jnp
from jax import lax
from jax.sharding import PartitionSpec as P

HD = 64
X_SIZE = 4


def hi_rounds(n_hi):
    rounds = [[(0, 1)] + ([(0, n_hi - 1)] if n_hi > 2 else [])]
    if n_hi > 3:
        rounds.append([(1, 2)])
    return rounds


def shift_perm(n, shift):
    return [(i, (i + shift) % n) for i in range(n)]


def pick(stacked, index):
    return lax.dynamic_index_in_dim(stacked, index, axis=0, keepdims=False)


def seg_broadcast(value, n_seg):
    seg = lax.axis_index("segment")
    n_hi = n_seg // X_SIZE
    x = seg % X_SIZE
    zh = seg // X_SIZE
    quarter = value.shape[1] // X_SIZE
    pieces = value.reshape(value.shape[0], X_SIZE, quarter, value.shape[2])
    mine = pieces[:, 0]
    for k in range(1, X_SIZE):
        got = lax.ppermute(pieces[:, k], "segment", [(0, k)])
        mine = jnp.where(seg == k, got, mine)
    for pairs in hi_rounds(n_hi):
        nxt = mine
        for a, b in pairs:
            perm = [(a * X_SIZE + c, b * X_SIZE + c) for c in range(X_SIZE)]
            got = lax.ppermute(mine, "segment", perm)
            nxt = jnp.where(zh == b, got, nxt)
        mine = nxt
    parts = [mine]
    for k in range(1, X_SIZE):
        perm = [(z * X_SIZE + c, z * X_SIZE + (c + k) % X_SIZE) for z in range(n_hi) for c in range(X_SIZE)]
        parts.append(lax.ppermute(mine, "segment", perm))
    stacked = jnp.stack(parts)
    full = jnp.stack([pick(stacked, (x - j) % X_SIZE) for j in range(X_SIZE)], axis=1)
    return full.reshape(value.shape)


def seg_reduce(value, n_seg):
    seg = lax.axis_index("segment")
    n_hi = n_seg // X_SIZE
    x = seg % X_SIZE
    zh = seg // X_SIZE
    quarter = value.shape[1] // X_SIZE
    pieces = value.reshape(value.shape[0], X_SIZE, quarter, value.shape[2])
    mine = pick(jnp.moveaxis(pieces, 1, 0), x)
    for k in range(1, X_SIZE):
        send = pick(jnp.moveaxis(pieces, 1, 0), (x + k) % X_SIZE)
        perm = [(z * X_SIZE + c, z * X_SIZE + (c + k) % X_SIZE) for z in range(n_hi) for c in range(X_SIZE)]
        mine = mine + lax.ppermute(send, "segment", perm)
    for pairs in reversed(hi_rounds(n_hi)):
        acc = mine
        for a, b in pairs:
            perm = [(b * X_SIZE + c, a * X_SIZE + c) for c in range(X_SIZE)]
            got = lax.ppermute(mine, "segment", perm)
            acc = acc + jnp.where(zh == a, got, jnp.zeros_like(got))
        mine = acc
    parts = [mine]
    for k in range(1, X_SIZE):
        parts.append(lax.ppermute(mine, "segment", [(k, 0)]))
    return jnp.stack(parts, axis=1).reshape(value.shape)


def tensor_gather(chunk, n_tensor):
    tix = lax.axis_index("tensor")
    core = tix % 2
    y = tix // 2
    n_y = n_tensor // 2
    other = lax.ppermute(chunk, "tensor", [(i, i ^ 1) for i in range(n_tensor)])
    block = jnp.where(core == 0, jnp.concatenate([chunk, other], axis=2),
                      jnp.concatenate([other, chunk], axis=2))
    half = n_y // 2
    ring = [(2 * j, 2 * ((j + 1) % n_y)) for j in range(n_y)]
    ring += [(2 * j + 1, 2 * ((j - 1) % n_y) + 1) for j in range(n_y)]
    collected = []
    cur = block
    for _ in range(half):
        cur = lax.ppermute(cur, "tensor", ring)
        collected.append(cur)
    mine = jnp.stack(collected)
    theirs = lax.ppermute(mine, "tensor", [(i, i ^ 1) for i in range(n_tensor)])
    down = jnp.where(core == 0, mine, theirs)
    up = jnp.where(core == 0, theirs, mine)
    n_up = n_y - 1 - half
    rel = [block] + [up[r - 1] for r in range(1, n_up + 1)] + [down[n_y - r - 1] for r in range(n_up + 1, n_y)]
    stacked = jnp.stack(rel)
    return jnp.concatenate([pick(stacked, (j - y) % n_y) for j in range(n_y)], axis=2)


def shards(inbound, weights, cotangent):
    n_seg = lax.axis_size("segment")
    n_dp = lax.axis_size("dp")
    n_tensor = lax.axis_size("tensor")
    seg = lax.axis_index("segment")
    tix = lax.axis_index("tensor")

    states = inbound[0]
    micro_count, row_count, model_width = states.shape
    layer = weights[0]
    feat_width = layer.shape[2]
    head_count = feat_width // HD
    scale = HD ** (-0.5)
    rows = micro_count * row_count

    query = jnp.dot(
        states.reshape(rows, model_width), layer[:, 0, :], preferred_element_type=jnp.float32
    ).astype(jnp.bfloat16)
    query = query.reshape(micro_count, row_count, feat_width)
    pair = jnp.stack([query, cotangent[0]])
    slots = [pair] + [lax.ppermute(pair, "dp", shift_perm(n_dp, k)) for k in range(1, n_dp)]
    slots = jnp.stack(slots)
    dix = lax.axis_index("dp")
    slots = jnp.stack([pick(slots, (dix - j) % n_dp) for j in range(n_dp)])
    query_heads = slots[:, 0].reshape(n_dp, micro_count, row_count, head_count, HD)
    grad_heads = slots[:, 1].reshape(n_dp, micro_count, row_count, head_count, HD)

    chunk_width = model_width // n_tensor
    chunk = lax.dynamic_slice_in_dim(states, tix * chunk_width, chunk_width, axis=2)
    chunk = seg_broadcast(chunk, n_seg)
    encoded = tensor_gather(chunk, n_tensor)

    pair_weights = layer[:, 1:, :].reshape(model_width, 2 * feat_width)
    keyval = jnp.dot(
        encoded.reshape(rows, model_width), pair_weights, preferred_element_type=jnp.float32
    ).astype(jnp.bfloat16)
    keyval = keyval.reshape(micro_count, row_count, 2, head_count, HD)
    key_heads = keyval[:, :, 0]
    value_heads = keyval[:, :, 1]

    scores = (
        jnp.einsum("jmqhe,mkhe->mhjqk", query_heads, key_heads, preferred_element_type=jnp.float32)
        * scale
    )
    prob_grad = jnp.einsum(
        "jmqhe,mkhe->mhjqk", grad_heads, value_heads, preferred_element_type=jnp.float32
    )
    local_peak = jnp.max(scores, axis=-1)
    local_exp = jnp.exp(scores - local_peak[..., None])
    local_sum = jnp.sum(local_exp, axis=-1)
    local_delta = jnp.sum(local_exp * prob_grad, axis=-1)
    stats = jnp.stack([local_peak, local_sum, local_delta])
    all_stats = jnp.stack(
        [stats] + [lax.ppermute(stats, "dp", shift_perm(n_dp, k)) for k in range(1, n_dp)]
    )
    peaks = all_stats[:, 0]
    peak = jnp.max(peaks, axis=0)
    weight = jnp.exp(peaks - peak[None])
    total = jnp.sum(all_stats[:, 1] * weight, axis=0)
    row_delta = jnp.sum(all_stats[:, 2] * weight, axis=0) / total

    attend_prob = jnp.exp(scores - peak[..., None]) / total[..., None]
    prob_rounded = attend_prob.astype(jnp.bfloat16)
    score_grad = (attend_prob * (prob_grad - row_delta[..., None]) * scale).astype(jnp.bfloat16)

    context_part = jnp.einsum(
        "mhjqk,mkhe->jmqhe", prob_rounded, value_heads, preferred_element_type=jnp.float32
    ).reshape(n_dp, micro_count, row_count, feat_width)
    context = pick(context_part, dix)
    for k in range(1, n_dp):
        send = pick(context_part, (dix - k) % n_dp)
        context = context + lax.ppermute(send, "dp", shift_perm(n_dp, -k))
    context = context.astype(jnp.bfloat16)

    key_grad = jnp.einsum(
        "mhjqk,jmqhe->mkhe", score_grad, query_heads, preferred_element_type=jnp.float32
    ).astype(jnp.bfloat16)
    value_grad = jnp.einsum(
        "mhjqk,jmqhe->mkhe", prob_rounded, grad_heads, preferred_element_type=jnp.float32
    ).astype(jnp.bfloat16)
    joined = jnp.stack(
        [key_grad.reshape(rows, feat_width), value_grad.reshape(rows, feat_width)], axis=1
    ).reshape(rows, 2 * feat_width)
    head_terms = jnp.einsum(
        "rc,dc->rd", joined, pair_weights, preferred_element_type=jnp.float32
    ).astype(jnp.bfloat16)
    head_terms = head_terms.reshape(micro_count, row_count, model_width)
    heads_total = lax.psum_scatter(head_terms, "tensor", scatter_dimension=2, tiled=True).astype(
        jnp.float32
    )
    heads_total = jnp.where(seg > 0, heads_total, jnp.zeros_like(heads_total))
    sections = seg_reduce(heads_total, n_seg)
    encoder_grad = (sections + cotangent[0].astype(jnp.float32)).astype(jnp.bfloat16)
    result = jnp.where(seg == 0, encoder_grad, context)
    return result[None]


def solution(mesh):
    placed = (
        P("segment", None, "dp", None),
        P("segment", None, None, "tensor"),
        P("segment", None, "dp", "tensor"),
    )
    return jax.shard_map(
        shards,
        mesh=mesh,
        in_specs=placed,
        out_specs=P("segment", None, "dp", "tensor"),
        check_vma=False,
    )
```

```python
import jax
import jax.numpy as jnp
from jax import lax
from jax.sharding import PartitionSpec as P

HD = 64
X_SIZE = 4


def hi_rounds(n_hi):
    rounds = [[(0, 1)] + ([(0, n_hi - 1)] if n_hi > 2 else [])]
    if n_hi > 3:
        rounds.append([(1, 2)])
    return rounds


def shift_perm(n, shift):
    return [(i, (i + shift) % n) for i in range(n)]


def pick(stacked, index):
    return lax.dynamic_index_in_dim(stacked, index, axis=0, keepdims=False)


def seg_broadcast(value, n_seg):
    seg = lax.axis_index("segment")
    n_hi = n_seg // X_SIZE
    x = seg % X_SIZE
    zh = seg // X_SIZE
    quarter = value.shape[1] // X_SIZE
    pieces = value.reshape(value.shape[0], X_SIZE, quarter, value.shape[2])
    mine = pieces[:, 0]
    for k in range(1, X_SIZE):
        got = lax.ppermute(pieces[:, k], "segment", [(0, k)])
        mine = jnp.where(seg == k, got, mine)
    for pairs in hi_rounds(n_hi):
        nxt = mine
        for a, b in pairs:
            perm = [(a * X_SIZE + c, b * X_SIZE + c) for c in range(X_SIZE)]
            got = lax.ppermute(mine, "segment", perm)
            nxt = jnp.where(zh == b, got, nxt)
        mine = nxt
    parts = [mine]
    for k in range(1, X_SIZE):
        perm = [(z * X_SIZE + c, z * X_SIZE + (c + k) % X_SIZE) for z in range(n_hi) for c in range(X_SIZE)]
        parts.append(lax.ppermute(mine, "segment", perm))
    stacked = jnp.stack(parts)
    full = jnp.stack([pick(stacked, (x - j) % X_SIZE) for j in range(X_SIZE)], axis=1)
    return full.reshape(value.shape)


def seg_reduce(value, n_seg):
    seg = lax.axis_index("segment")
    n_hi = n_seg // X_SIZE
    x = seg % X_SIZE
    zh = seg // X_SIZE
    quarter = value.shape[1] // X_SIZE
    pieces = value.reshape(value.shape[0], X_SIZE, quarter, value.shape[2])
    mine = pick(jnp.moveaxis(pieces, 1, 0), x)
    for k in range(1, X_SIZE):
        send = pick(jnp.moveaxis(pieces, 1, 0), (x + k) % X_SIZE)
        perm = [(z * X_SIZE + c, z * X_SIZE + (c + k) % X_SIZE) for z in range(n_hi) for c in range(X_SIZE)]
        mine = mine + lax.ppermute(send, "segment", perm)
    for pairs in reversed(hi_rounds(n_hi)):
        acc = mine
        for a, b in pairs:
            perm = [(b * X_SIZE + c, a * X_SIZE + c) for c in range(X_SIZE)]
            got = lax.ppermute(mine, "segment", perm)
            acc = acc + jnp.where(zh == a, got, jnp.zeros_like(got))
        mine = acc
    parts = [mine]
    for k in range(1, X_SIZE):
        parts.append(lax.ppermute(mine, "segment", [(k, 0)]))
    return jnp.stack(parts, axis=1).reshape(value.shape)


def tensor_gather(chunk, n_tensor):
    tix = lax.axis_index("tensor")
    core = tix % 2
    y = tix // 2
    n_y = n_tensor // 2
    other = lax.ppermute(chunk, "tensor", [(i, i ^ 1) for i in range(n_tensor)])
    block = jnp.where(core == 0, jnp.concatenate([chunk, other], axis=2),
                      jnp.concatenate([other, chunk], axis=2))
    half = n_y // 2
    ring = [(2 * j, 2 * ((j + 1) % n_y)) for j in range(n_y)]
    ring += [(2 * j + 1, 2 * ((j - 1) % n_y) + 1) for j in range(n_y)]
    collected = []
    cur = block
    for _ in range(half):
        cur = lax.ppermute(cur, "tensor", ring)
        collected.append(cur)
    mine = jnp.stack(collected)
    theirs = lax.ppermute(mine, "tensor", [(i, i ^ 1) for i in range(n_tensor)])
    down = jnp.where(core == 0, mine, theirs)
    up = jnp.where(core == 0, theirs, mine)
    n_up = n_y - 1 - half
    rel = [block] + [up[r - 1] for r in range(1, n_up + 1)] + [down[n_y - r - 1] for r in range(n_up + 1, n_y)]
    stacked = jnp.stack(rel)
    return jnp.concatenate([pick(stacked, (j - y) % n_y) for j in range(n_y)], axis=2)


def dp_gather(value, n_dp):
    spread = jnp.broadcast_to(value[None], (n_dp,) + value.shape)
    return lax.all_to_all(spread, "dp", 0, 0, tiled=False)


def shards(inbound, weights, cotangent):
    n_seg = lax.axis_size("segment")
    n_dp = lax.axis_size("dp")
    n_tensor = lax.axis_size("tensor")
    seg = lax.axis_index("segment")
    tix = lax.axis_index("tensor")

    states = inbound[0]
    micro_count, row_count, model_width = states.shape
    layer = weights[0]
    feat_width = layer.shape[2]
    head_count = feat_width // HD
    scale = HD ** (-0.5)
    rows = micro_count * row_count

    query = jnp.dot(
        states.reshape(rows, model_width), layer[:, 0, :], preferred_element_type=jnp.float32
    ).astype(jnp.bfloat16)
    query = query.reshape(micro_count, row_count, feat_width)
    pair = jnp.stack([query, cotangent[0]])
    slots = dp_gather(pair, n_dp)
    query_heads = slots[:, 0].reshape(n_dp, micro_count, row_count, head_count, HD)
    grad_heads = slots[:, 1].reshape(n_dp, micro_count, row_count, head_count, HD)

    chunk_width = model_width // n_tensor
    chunk = lax.dynamic_slice_in_dim(states, tix * chunk_width, chunk_width, axis=2)
    chunk = seg_broadcast(chunk, n_seg)
    spread = jnp.broadcast_to(chunk[None], (n_tensor,) + chunk.shape)
    encoded = lax.all_to_all(spread, "tensor", 0, 0, tiled=False)
    encoded = jnp.moveaxis(encoded, 0, 2).reshape(micro_count, row_count, model_width)

    flat_enc = encoded.reshape(rows, model_width)
    key_heads = jnp.dot(flat_enc, layer[:, 1, :], preferred_element_type=jnp.float32).astype(
        jnp.bfloat16
    ).reshape(micro_count, row_count, head_count, HD)
    value_heads = jnp.dot(flat_enc, layer[:, 2, :], preferred_element_type=jnp.float32).astype(
        jnp.bfloat16
    ).reshape(micro_count, row_count, head_count, HD)

    scores = (
        jnp.einsum("jmqhe,mkhe->mhjqk", query_heads, key_heads, preferred_element_type=jnp.float32)
        * scale
    )
    prob_grad = jnp.einsum(
        "jmqhe,mkhe->mhjqk", grad_heads, value_heads, preferred_element_type=jnp.float32
    )
    local_peak = jnp.max(scores, axis=-1)
    local_exp = jnp.exp(scores - local_peak[..., None])
    local_sum = jnp.sum(local_exp, axis=-1)
    local_delta = jnp.sum(local_exp * prob_grad, axis=-1)
    stats = jnp.stack([local_peak, local_sum, local_delta])
    all_stats = dp_gather(stats, n_dp)
    peaks = all_stats[:, 0]
    peak = jnp.max(peaks, axis=0)
    weight = jnp.exp(peaks - peak[None])
    total = jnp.sum(all_stats[:, 1] * weight, axis=0)
    row_delta = jnp.sum(all_stats[:, 2] * weight, axis=0) / total

    attend_prob = jnp.exp(scores - peak[..., None]) / total[..., None]
    prob_rounded = attend_prob.astype(jnp.bfloat16)
    score_grad = (attend_prob * (prob_grad - row_delta[..., None]) * scale).astype(jnp.bfloat16)

    context_part = jnp.einsum(
        "mhjqk,mkhe->jmqhe", prob_rounded, value_heads, preferred_element_type=jnp.float32
    ).reshape(n_dp, micro_count, row_count, feat_width)
    context = jnp.sum(lax.all_to_all(context_part, "dp", 0, 0, tiled=False), axis=0)
    context = context.astype(jnp.bfloat16)

    key_grad = jnp.einsum(
        "mhjqk,jmqhe->mkhe", score_grad, query_heads, preferred_element_type=jnp.float32
    ).astype(jnp.bfloat16)
    value_grad = jnp.einsum(
        "mhjqk,jmqhe->mkhe", prob_rounded, grad_heads, preferred_element_type=jnp.float32
    ).astype(jnp.bfloat16)
    head_terms = (
        jnp.einsum("rc,dc->rd", key_grad.reshape(rows, feat_width), layer[:, 1, :],
                   preferred_element_type=jnp.float32)
        + jnp.einsum("rc,dc->rd", value_grad.reshape(rows, feat_width), layer[:, 2, :],
                     preferred_element_type=jnp.float32)
    ).astype(jnp.bfloat16)
    head_terms = head_terms.reshape(micro_count, row_count, n_tensor, chunk_width)
    head_terms = jnp.moveaxis(head_terms, 2, 0)
    heads_total = jnp.sum(
        lax.all_to_all(head_terms, "tensor", 0, 0, tiled=False).astype(jnp.float32), axis=0
    )
    heads_total = jnp.where(seg > 0, heads_total, jnp.zeros_like(heads_total))
    sections = seg_reduce(heads_total, n_seg)
    encoder_grad = (sections + cotangent[0].astype(jnp.float32)).astype(jnp.bfloat16)
    result = jnp.where(seg == 0, encoder_grad, context)
    return result[None]


def solution(mesh):
    placed = (
        P("segment", None, "dp", None),
        P("segment", None, None, "tensor"),
        P("segment", None, "dp", "tensor"),
    )
    return jax.shard_map(
        shards,
        mesh=mesh,
        in_specs=placed,
        out_specs=P("segment", None, "dp", "tensor"),
        check_vma=False,
    )
```

```python
import jax
import jax.numpy as jnp
from jax import lax
from jax.sharding import Mesh, PartitionSpec as P

HD = 64
X_SIZE = 4
SEG = ("zh", "x")
TEN = ("ty", "tc")


def hi_rounds(n_hi):
    rounds = [[(0, 1)] + ([(0, n_hi - 1)] if n_hi > 2 else [])]
    if n_hi > 3:
        rounds.append([(1, 2)])
    return rounds


def gather_axis(value, axis, n):
    spread = jnp.broadcast_to(value[None], (n,) + value.shape)
    return lax.all_to_all(spread, axis, 0, 0, tiled=False)


def seg_broadcast(value, n_hi, n_x):
    x = lax.axis_index("x")
    zh = lax.axis_index("zh")
    quarter = value.shape[1] // n_x
    pieces = value.reshape(value.shape[0], n_x, quarter, value.shape[2])
    mine = pieces[:, 0]
    for k in range(1, n_x):
        got = lax.ppermute(pieces[:, k], "x", [(0, k)])
        mine = jnp.where(x == k, got, mine)
    for pairs in hi_rounds(n_hi):
        nxt = mine
        for a, b in pairs:
            got = lax.ppermute(mine, "zh", [(a, b)])
            nxt = jnp.where(zh == b, got, nxt)
        mine = nxt
    full = gather_axis(mine, "x", n_x)
    return jnp.moveaxis(full, 0, 1).reshape(value.shape)


def seg_reduce(value, n_hi, n_x):
    zh = lax.axis_index("zh")
    quarter = value.shape[1] // n_x
    pieces = jnp.moveaxis(value.reshape(value.shape[0], n_x, quarter, value.shape[2]), 1, 0)
    mine = jnp.sum(lax.all_to_all(pieces, "x", 0, 0, tiled=False), axis=0)
    for pairs in reversed(hi_rounds(n_hi)):
        acc = mine
        for a, b in pairs:
            got = lax.ppermute(mine, "zh", [(b, a)])
            acc = acc + jnp.where(zh == a, got, jnp.zeros_like(got))
        mine = acc
    parts = [mine]
    for k in range(1, n_x):
        parts.append(lax.ppermute(mine, "x", [(k, 0)]))
    return jnp.stack(parts, axis=1).reshape(value.shape)


def shards(inbound, weights, cotangent):
    n_hi = lax.axis_size("zh")
    n_x = lax.axis_size("x")
    n_dp = lax.axis_size("dp")
    n_y = lax.axis_size("ty")
    n_c = lax.axis_size("tc")
    n_tensor = n_y * n_c
    seg = lax.axis_index("zh") * n_x + lax.axis_index("x")
    core = lax.axis_index("tc")
    tix = lax.axis_index("ty") * n_c + core

    states = inbound[0]
    micro_count, row_count, model_width = states.shape
    layer = weights[0]
    feat_width = layer.shape[2]
    head_count = feat_width // HD
    scale = HD ** (-0.5)
    rows = micro_count * row_count
    chunk_width = model_width // n_tensor

    query = jnp.dot(
        states.reshape(rows, model_width), layer[:, 0, :], preferred_element_type=jnp.float32
    ).astype(jnp.bfloat16)
    query = query.reshape(micro_count, row_count, feat_width)
    slots = gather_axis(jnp.stack([query, cotangent[0]]), "dp", n_dp)
    query_heads = slots[:, 0].reshape(n_dp, micro_count, row_count, head_count, HD)
    grad_heads = slots[:, 1].reshape(n_dp, micro_count, row_count, head_count, HD)

    chunk = lax.dynamic_slice_in_dim(states, tix * chunk_width, chunk_width, axis=2)
    chunk = seg_broadcast(chunk, n_hi, n_x)
    own = gather_axis(chunk, "ty", n_y)
    both = gather_axis(own, "tc", n_c)
    encoded = jnp.transpose(both, (2, 3, 1, 0, 4)).reshape(micro_count, row_count, model_width)

    flat_enc = encoded.reshape(rows, model_width)
    key_heads = jnp.dot(flat_enc, layer[:, 1, :], preferred_element_type=jnp.float32).astype(
        jnp.bfloat16
    ).reshape(micro_count, row_count, head_count, HD)
    value_heads = jnp.dot(flat_enc, layer[:, 2, :], preferred_element_type=jnp.float32).astype(
        jnp.bfloat16
    ).reshape(micro_count, row_count, head_count, HD)

    scores = (
        jnp.einsum("jmqhe,mkhe->mhjqk", query_heads, key_heads, preferred_element_type=jnp.float32)
        * scale
    )
    prob_grad = jnp.einsum(
        "jmqhe,mkhe->mhjqk", grad_heads, value_heads, preferred_element_type=jnp.float32
    )
    local_peak = jnp.max(scores, axis=-1)
    local_exp = jnp.exp(scores - local_peak[..., None])
    local_sum = jnp.sum(local_exp, axis=-1)
    local_delta = jnp.sum(local_exp * prob_grad, axis=-1)
    stats = jnp.stack([local_peak, local_sum, local_delta])
    all_stats = gather_axis(stats, "dp", n_dp)
    peaks = all_stats[:, 0]
    peak = jnp.max(peaks, axis=0)
    weight = jnp.exp(peaks - peak[None])
    total = jnp.sum(all_stats[:, 1] * weight, axis=0)
    row_delta = jnp.sum(all_stats[:, 2] * weight, axis=0) / total

    attend_prob = jnp.exp(scores - peak[..., None]) / total[..., None]
    prob_rounded = attend_prob.astype(jnp.bfloat16)
    score_grad = (attend_prob * (prob_grad - row_delta[..., None]) * scale).astype(jnp.bfloat16)

    context_part = jnp.einsum(
        "mhjqk,mkhe->jmqhe", prob_rounded, value_heads, preferred_element_type=jnp.float32
    ).reshape(n_dp, micro_count, row_count, feat_width)
    context = jnp.sum(lax.all_to_all(context_part, "dp", 0, 0, tiled=False), axis=0)
    context = context.astype(jnp.bfloat16)

    key_grad = jnp.einsum(
        "mhjqk,jmqhe->mkhe", score_grad, query_heads, preferred_element_type=jnp.float32
    ).astype(jnp.bfloat16)
    value_grad = jnp.einsum(
        "mhjqk,jmqhe->mkhe", prob_rounded, grad_heads, preferred_element_type=jnp.float32
    ).astype(jnp.bfloat16)
    head_terms = (
        jnp.einsum("rc,dc->rd", key_grad.reshape(rows, feat_width), layer[:, 1, :],
                   preferred_element_type=jnp.float32)
        + jnp.einsum("rc,dc->rd", value_grad.reshape(rows, feat_width), layer[:, 2, :],
                     preferred_element_type=jnp.float32)
    ).astype(jnp.bfloat16)
    head_terms = head_terms.reshape(micro_count, row_count, n_y, n_c, chunk_width)
    head_terms = jnp.transpose(head_terms, (3, 2, 0, 1, 4))
    pair_sum = jnp.sum(
        lax.all_to_all(head_terms, "tc", 0, 0, tiled=False).astype(jnp.float32), axis=0
    ).astype(jnp.bfloat16)
    heads_total = jnp.sum(
        lax.all_to_all(pair_sum, "ty", 0, 0, tiled=False).astype(jnp.float32), axis=0
    )
    heads_total = jnp.where(seg > 0, heads_total, jnp.zeros_like(heads_total))
    sections = seg_reduce(heads_total, n_hi, n_x)
    encoder_grad = (sections + cotangent[0].astype(jnp.float32)).astype(jnp.bfloat16)
    result = jnp.where(seg == 0, encoder_grad, context)
    return result[None]


def solution(mesh):
    n_seg, n_dp, n_tensor = (mesh.shape[a] for a in ("segment", "dp", "tensor"))
    sub = Mesh(
        mesh.devices.reshape(n_seg // X_SIZE, X_SIZE, n_dp, n_tensor // 2, 2),
        SEG + ("dp",) + TEN,
    )
    placed = (
        P(SEG, None, "dp", None),
        P(SEG, None, None, TEN),
        P(SEG, None, "dp", TEN),
    )
    return jax.shard_map(
        shards,
        mesh=sub,
        in_specs=placed,
        out_specs=P(SEG, None, "dp", TEN),
        check_vma=False,
    )
```

```python
import jax
import jax.numpy as jnp
from jax import lax
from jax.sharding import Mesh, PartitionSpec as P

HD = 64
X_SIZE = 4
SEG = ("zh", "x")
TEN = ("ty", "tc")


def hi_rounds(n_hi):
    rounds = [[(0, 1)] + ([(0, n_hi - 1)] if n_hi > 2 else [])]
    if n_hi > 3:
        rounds.append([(1, 2)])
    return rounds


def gather_axis(value, axis, n):
    spread = jnp.broadcast_to(value[None], (n,) + value.shape)
    return lax.all_to_all(spread, axis, 0, 0, tiled=False)


def seg_broadcast(value, n_hi, n_x):
    x = lax.axis_index("x")
    zh = lax.axis_index("zh")
    quarter = value.shape[1] // n_x
    pieces = value.reshape(value.shape[0], n_x, quarter, value.shape[2])
    mine = pieces[:, 0]
    for k in range(1, n_x):
        got = lax.ppermute(pieces[:, k], "x", [(0, k)])
        mine = jnp.where(x == k, got, mine)
    out = mine
    for b in range(1, n_hi):
        got = lax.ppermute(mine, "zh", [(0, b)])
        out = jnp.where(zh == b, got, out)
    return out


def seg_reduce(mine, n_hi, n_x):
    zh = lax.axis_index("zh")
    acc = mine
    for b in range(1, n_hi):
        got = lax.ppermute(mine, "zh", [(b, 0)])
        acc = acc + got
    acc = jnp.where(zh == 0, acc, mine)
    parts = [acc]
    for k in range(1, n_x):
        parts.append(lax.ppermute(acc, "x", [(k, 0)]))
    stacked = jnp.stack(parts, axis=1)
    return stacked.reshape(stacked.shape[0], -1, stacked.shape[-1])


def shards(inbound, weights, cotangent):
    n_hi = lax.axis_size("zh")
    n_x = lax.axis_size("x")
    n_dp = lax.axis_size("dp")
    n_y = lax.axis_size("ty")
    n_c = lax.axis_size("tc")
    n_tensor = n_y * n_c
    seg = lax.axis_index("zh") * n_x + lax.axis_index("x")
    core = lax.axis_index("tc")
    tix = lax.axis_index("ty") * n_c + core

    states = inbound[0]
    micro_count, row_count, model_width = states.shape
    layer = weights[0]
    feat_width = layer.shape[2]
    head_count = feat_width // HD
    scale = HD ** (-0.5)
    rows = micro_count * row_count
    chunk_width = model_width // n_tensor

    query = jnp.dot(
        states.reshape(rows, model_width), layer[:, 0, :], preferred_element_type=jnp.float32
    ).astype(jnp.bfloat16)
    query = query.reshape(micro_count, row_count, feat_width)
    slots = gather_axis(jnp.stack([query, cotangent[0]]), "dp", n_dp)
    query_heads = slots[:, 0].reshape(n_dp, micro_count, row_count, head_count, HD)
    grad_heads = slots[:, 1].reshape(n_dp, micro_count, row_count, head_count, HD)

    chunk = lax.dynamic_slice_in_dim(states, tix * chunk_width, chunk_width, axis=2)
    piece = seg_broadcast(chunk, n_hi, n_x)
    own = gather_axis(piece, ("x", "ty"), n_x * n_y)
    both = gather_axis(own, "tc", n_c)
    both = both.reshape(n_c, n_x, n_y, micro_count, row_count // n_x, chunk_width)
    encoded = jnp.transpose(both, (3, 1, 4, 2, 0, 5)).reshape(micro_count, row_count, model_width)

    flat_enc = encoded.reshape(rows, model_width)
    key_heads = jnp.dot(flat_enc, layer[:, 1, :], preferred_element_type=jnp.float32).astype(
        jnp.bfloat16
    ).reshape(micro_count, row_count, head_count, HD)
    value_heads = jnp.dot(flat_enc, layer[:, 2, :], preferred_element_type=jnp.float32).astype(
        jnp.bfloat16
    ).reshape(micro_count, row_count, head_count, HD)

    scores = (
        jnp.einsum("jmqhe,mkhe->mhjqk", query_heads, key_heads, preferred_element_type=jnp.float32)
        * scale
    )
    prob_grad = jnp.einsum(
        "jmqhe,mkhe->mhjqk", grad_heads, value_heads, preferred_element_type=jnp.float32
    )
    local_peak = jnp.max(scores, axis=-1)
    local_exp = jnp.exp(scores - local_peak[..., None])
    local_sum = jnp.sum(local_exp, axis=-1)
    local_delta = jnp.sum(local_exp * prob_grad, axis=-1)
    stats = jnp.stack([local_peak, local_sum, local_delta])
    all_stats = gather_axis(stats, "dp", n_dp)
    peaks = all_stats[:, 0]
    peak = jnp.max(peaks, axis=0)
    weight = jnp.exp(peaks - peak[None])
    total = jnp.sum(all_stats[:, 1] * weight, axis=0)
    row_delta = jnp.sum(all_stats[:, 2] * weight, axis=0) / total

    attend_prob = jnp.exp(scores - peak[..., None]) / total[..., None]
    prob_rounded = attend_prob.astype(jnp.bfloat16)
    score_grad = (attend_prob * (prob_grad - row_delta[..., None]) * scale).astype(jnp.bfloat16)

    context_part = jnp.einsum(
        "mhjqk,mkhe->jmqhe", prob_rounded, value_heads, preferred_element_type=jnp.float32
    ).reshape(n_dp, micro_count, row_count, feat_width)
    context = jnp.sum(lax.all_to_all(context_part, "dp", 0, 0, tiled=False), axis=0)
    context = context.astype(jnp.bfloat16)

    key_grad = jnp.einsum(
        "mhjqk,jmqhe->mkhe", score_grad, query_heads, preferred_element_type=jnp.float32
    ).astype(jnp.bfloat16)
    value_grad = jnp.einsum(
        "mhjqk,jmqhe->mkhe", prob_rounded, grad_heads, preferred_element_type=jnp.float32
    ).astype(jnp.bfloat16)
    head_terms = (
        jnp.einsum("rc,dc->rd", key_grad.reshape(rows, feat_width), layer[:, 1, :],
                   preferred_element_type=jnp.float32)
        + jnp.einsum("rc,dc->rd", value_grad.reshape(rows, feat_width), layer[:, 2, :],
                     preferred_element_type=jnp.float32)
    ).astype(jnp.bfloat16)
    head_terms = head_terms.reshape(micro_count, row_count, n_y, n_c, chunk_width)
    head_terms = jnp.transpose(head_terms, (3, 2, 0, 1, 4))
    pair_sum = jnp.sum(
        lax.all_to_all(head_terms, "tc", 0, 0, tiled=False).astype(jnp.float32), axis=0
    ).astype(jnp.bfloat16)
    pair_sum = jnp.where(seg > 0, pair_sum, jnp.zeros_like(pair_sum))
    quarter = row_count // n_x
    pair_sum = pair_sum.reshape(n_y, micro_count, n_x, quarter, chunk_width)
    pair_sum = jnp.transpose(pair_sum, (2, 0, 1, 3, 4)).reshape(n_x * n_y, micro_count, quarter, chunk_width)
    heads_total = jnp.sum(
        lax.all_to_all(pair_sum, ("x", "ty"), 0, 0, tiled=False).astype(jnp.float32), axis=0
    )
    sections = seg_reduce(heads_total, n_hi, n_x)
    encoder_grad = (sections + cotangent[0].astype(jnp.float32)).astype(jnp.bfloat16)
    result = jnp.where(seg == 0, encoder_grad, context)
    return result[None]


def solution(mesh):
    n_seg, n_dp, n_tensor = (mesh.shape[a] for a in ("segment", "dp", "tensor"))
    sub = Mesh(
        mesh.devices.reshape(n_seg // X_SIZE, X_SIZE, n_dp, n_tensor // 2, 2),
        SEG + ("dp",) + TEN,
    )
    placed = (
        P(SEG, None, "dp", None),
        P(SEG, None, None, TEN),
        P(SEG, None, "dp", TEN),
    )
    return jax.shard_map(
        shards,
        mesh=sub,
        in_specs=placed,
        out_specs=P(SEG, None, "dp", TEN),
        check_vma=False,
    )
```

```python
import jax
import jax.numpy as jnp
from jax import lax
from jax.sharding import Mesh, PartitionSpec as P

HD = 64
X_SIZE = 4
SEG = ("zh", "x")
TEN = ("ty", "tc")


def hi_rounds(n_hi):
    rounds = [[(0, 1)] + ([(0, n_hi - 1)] if n_hi > 2 else [])]
    if n_hi > 3:
        rounds.append([(1, 2)])
    return rounds


def gather_axis(value, axis, n):
    spread = jnp.broadcast_to(value[None], (n,) + value.shape)
    return lax.all_to_all(spread, axis, 0, 0, tiled=False)


def seg_broadcast(value, n_hi, n_x):
    x = lax.axis_index("x")
    zh = lax.axis_index("zh")
    quarter = value.shape[1] // n_x
    pieces = value.reshape(value.shape[0], n_x, quarter, value.shape[2])
    mine = pieces[:, 0]
    for k in range(1, n_x):
        got = lax.ppermute(pieces[:, k], "x", [(0, k)])
        mine = jnp.where(x == k, got, mine)
    out = mine
    for b in range(1, n_hi):
        got = lax.ppermute(mine, "zh", [(0, b)])
        out = jnp.where(zh == b, got, out)
    return out


def seg_reduce(mine, n_hi, n_x):
    zh = lax.axis_index("zh")
    sent = mine.astype(jnp.bfloat16)
    acc = mine
    for b in range(1, n_hi):
        got = lax.ppermute(sent, "zh", [(b, 0)])
        acc = acc + got.astype(jnp.float32)
    acc = jnp.where(zh == 0, acc, mine)
    parts = [acc]
    sent = acc.astype(jnp.bfloat16)
    for k in range(1, n_x):
        parts.append(lax.ppermute(sent, "x", [(k, 0)]).astype(jnp.float32))
    stacked = jnp.stack(parts, axis=1)
    return stacked.reshape(stacked.shape[0], -1, stacked.shape[-1])


def shards(inbound, weights, cotangent):
    n_hi = lax.axis_size("zh")
    n_x = lax.axis_size("x")
    n_dp = lax.axis_size("dp")
    n_y = lax.axis_size("ty")
    n_c = lax.axis_size("tc")
    n_tensor = n_y * n_c
    seg = lax.axis_index("zh") * n_x + lax.axis_index("x")
    core = lax.axis_index("tc")
    tix = lax.axis_index("ty") * n_c + core

    states = inbound[0]
    micro_count, row_count, model_width = states.shape
    layer = weights[0]
    feat_width = layer.shape[2]
    head_count = feat_width // HD
    scale = HD ** (-0.5)
    rows = micro_count * row_count
    chunk_width = model_width // n_tensor

    query = jnp.dot(
        states.reshape(rows, model_width), layer[:, 0, :], preferred_element_type=jnp.float32
    ).astype(jnp.bfloat16)
    query = query.reshape(micro_count, row_count, feat_width)
    slots = gather_axis(jnp.stack([query, cotangent[0]]), "dp", n_dp)

    chunk = lax.dynamic_slice_in_dim(states, tix * chunk_width, chunk_width, axis=2)
    piece = seg_broadcast(chunk, n_hi, n_x)
    slots, piece = lax.optimization_barrier((slots, piece))
    own = gather_axis(piece, ("x", "ty"), n_x * n_y)
    both = gather_axis(own, "tc", n_c)
    both = both.reshape(n_c, n_x, n_y, micro_count, row_count // n_x, chunk_width)
    encoded = jnp.transpose(both, (3, 1, 4, 2, 0, 5)).reshape(micro_count, row_count, model_width)

    query_heads = slots[:, 0].reshape(n_dp, micro_count, row_count, head_count, HD)
    grad_heads = slots[:, 1].reshape(n_dp, micro_count, row_count, head_count, HD)
    flat_enc = encoded.reshape(rows, model_width)
    key_heads = jnp.dot(flat_enc, layer[:, 1, :], preferred_element_type=jnp.float32).astype(
        jnp.bfloat16
    ).reshape(micro_count, row_count, head_count, HD)
    value_heads = jnp.dot(flat_enc, layer[:, 2, :], preferred_element_type=jnp.float32).astype(
        jnp.bfloat16
    ).reshape(micro_count, row_count, head_count, HD)

    scores = (
        jnp.einsum("jmqhe,mkhe->mhjqk", query_heads, key_heads, preferred_element_type=jnp.float32)
        * scale
    )
    prob_grad = jnp.einsum(
        "jmqhe,mkhe->mhjqk", grad_heads, value_heads, preferred_element_type=jnp.float32
    )
    local_peak = jnp.max(scores, axis=-1)
    local_exp = jnp.exp(scores - local_peak[..., None])
    local_sum = jnp.sum(local_exp, axis=-1)
    local_delta = jnp.sum(local_exp * prob_grad, axis=-1)
    stats = jnp.stack([local_peak, local_sum, local_delta])
    all_stats = gather_axis(stats, "dp", n_dp)
    peaks = all_stats[:, 0]
    peak = jnp.max(peaks, axis=0)
    weight = jnp.exp(peaks - peak[None])
    total = jnp.sum(all_stats[:, 1] * weight, axis=0)
    row_delta = jnp.sum(all_stats[:, 2] * weight, axis=0) / total

    attend_prob = jnp.exp(scores - peak[..., None]) / total[..., None]
    prob_rounded = attend_prob.astype(jnp.bfloat16)
    score_grad = (attend_prob * (prob_grad - row_delta[..., None]) * scale).astype(jnp.bfloat16)

    context_part = jnp.einsum(
        "mhjqk,mkhe->jmqhe", prob_rounded, value_heads, preferred_element_type=jnp.float32
    ).reshape(n_dp, micro_count, row_count, feat_width)
    context = jnp.sum(lax.all_to_all(context_part, "dp", 0, 0, tiled=False), axis=0)
    context = context.astype(jnp.bfloat16)

    key_grad = jnp.einsum(
        "mhjqk,jmqhe->mkhe", score_grad, query_heads, preferred_element_type=jnp.float32
    ).astype(jnp.bfloat16)
    value_grad = jnp.einsum(
        "mhjqk,jmqhe->mkhe", prob_rounded, grad_heads, preferred_element_type=jnp.float32
    ).astype(jnp.bfloat16)
    head_terms = (
        jnp.einsum("rc,dc->rd", key_grad.reshape(rows, feat_width), layer[:, 1, :],
                   preferred_element_type=jnp.float32)
        + jnp.einsum("rc,dc->rd", value_grad.reshape(rows, feat_width), layer[:, 2, :],
                     preferred_element_type=jnp.float32)
    ).astype(jnp.bfloat16)
    head_terms = head_terms.reshape(micro_count, row_count, n_y, n_c, chunk_width)
    pair_sum = jnp.sum(
        lax.all_to_all(head_terms, "tc", 3, 0, tiled=False).astype(jnp.float32), axis=0
    ).astype(jnp.bfloat16)
    pair_sum = jnp.moveaxis(pair_sum, 2, 0)
    pair_sum = jnp.where(seg > 0, pair_sum, jnp.zeros_like(pair_sum))
    quarter = row_count // n_x
    pair_sum = pair_sum.reshape(n_y, micro_count, n_x, quarter, chunk_width)
    pair_sum = jnp.transpose(pair_sum, (2, 0, 1, 3, 4)).reshape(n_x * n_y, micro_count, quarter, chunk_width)
    heads_total = jnp.sum(
        lax.all_to_all(pair_sum, ("x", "ty"), 0, 0, tiled=False).astype(jnp.float32), axis=0
    )
    sections = seg_reduce(heads_total, n_hi, n_x)
    encoder_grad = (sections + cotangent[0].astype(jnp.float32)).astype(jnp.bfloat16)
    result = jnp.where(seg == 0, encoder_grad, context)
    return result[None]


def solution(mesh):
    n_seg, n_dp, n_tensor = (mesh.shape[a] for a in ("segment", "dp", "tensor"))
    sub = Mesh(
        mesh.devices.reshape(n_seg // X_SIZE, X_SIZE, n_dp, n_tensor // 2, 2),
        SEG + ("dp",) + TEN,
    )
    placed = (
        P(SEG, None, "dp", None),
        P(SEG, None, None, TEN),
        P(SEG, None, "dp", TEN),
    )
    return jax.shard_map(
        shards,
        mesh=sub,
        in_specs=placed,
        out_specs=P(SEG, None, "dp", TEN),
        check_vma=False,
    )
```

```python
import jax
import jax.numpy as jnp
from jax import lax
from jax.sharding import Mesh, PartitionSpec as P

HD = 64
X_SIZE = 4
SEG = ("zh", "x")
TEN = ("ty", "tc")


def hi_rounds(n_hi):
    rounds = [[(0, 1)] + ([(0, n_hi - 1)] if n_hi > 2 else [])]
    if n_hi > 3:
        rounds.append([(1, 2)])
    return rounds


def gather_axis(value, axis, n):
    spread = jnp.broadcast_to(value[None], (n,) + value.shape)
    return lax.all_to_all(spread, axis, 0, 0, tiled=False)


def seg_broadcast(value, n_hi, n_x):
    x = lax.axis_index("x")
    zh = lax.axis_index("zh")
    quarter = value.shape[1] // n_x
    pieces = value.reshape(value.shape[0], n_x, quarter, value.shape[2])
    mine = pieces[:, 0]
    for k in range(1, n_x):
        got = lax.ppermute(pieces[:, k], "x", [(0, k)])
        mine = jnp.where(x == k, got, mine)
    out = mine
    for b in range(1, n_hi):
        got = lax.ppermute(mine, "zh", [(0, b)])
        out = jnp.where(zh == b, got, out)
    return out


def seg_reduce(mine, n_hi, n_x):
    zh = lax.axis_index("zh")
    sent = mine.astype(jnp.bfloat16)
    acc = mine
    for b in range(1, n_hi):
        got = lax.ppermute(sent, "zh", [(b, 0)])
        acc = acc + got.astype(jnp.float32)
    acc = jnp.where(zh == 0, acc, mine)
    parts = [acc]
    sent = acc.astype(jnp.bfloat16)
    for k in range(1, n_x):
        parts.append(lax.ppermute(sent, "x", [(k, 0)]).astype(jnp.float32))
    stacked = jnp.stack(parts, axis=1)
    return stacked.reshape(stacked.shape[0], -1, stacked.shape[-1])


def shards(inbound, weights, cotangent):
    n_hi = lax.axis_size("zh")
    n_x = lax.axis_size("x")
    n_dp = lax.axis_size("dp")
    n_y = lax.axis_size("ty")
    n_c = lax.axis_size("tc")
    n_tensor = n_y * n_c
    seg = lax.axis_index("zh") * n_x + lax.axis_index("x")
    core = lax.axis_index("tc")
    tix = lax.axis_index("ty") * n_c + core

    states = inbound[0]
    micro_count, row_count, model_width = states.shape
    layer = weights[0]
    feat_width = layer.shape[2]
    head_count = feat_width // HD
    scale = HD ** (-0.5)
    rows = micro_count * row_count
    chunk_width = model_width // n_tensor

    query = jnp.dot(
        states.reshape(rows, model_width), layer[:, 0, :], preferred_element_type=jnp.float32
    ).astype(jnp.bfloat16)
    query = query.reshape(micro_count, row_count, feat_width)
    slots = gather_axis(jnp.stack([query, cotangent[0]]), "dp", n_dp)

    chunk = lax.dynamic_slice_in_dim(states, tix * chunk_width, chunk_width, axis=2)
    piece = seg_broadcast(chunk, n_hi, n_x)
    slots, piece = lax.optimization_barrier((slots, piece))
    def chain(piece, slots, upstream):
        micro_count = 1
        rows = row_count
        own = gather_axis(piece, ("x", "ty"), n_x * n_y)
        both = gather_axis(own, "tc", n_c)
        both = both.reshape(n_c, n_x, n_y, micro_count, row_count // n_x, chunk_width)
        encoded = jnp.transpose(both, (3, 1, 4, 2, 0, 5)).reshape(micro_count, row_count, model_width)

        query_heads = slots[:, 0].reshape(n_dp, micro_count, row_count, head_count, HD)
        grad_heads = slots[:, 1].reshape(n_dp, micro_count, row_count, head_count, HD)
        flat_enc = encoded.reshape(rows, model_width)
        key_heads = jnp.dot(flat_enc, layer[:, 1, :], preferred_element_type=jnp.float32).astype(
            jnp.bfloat16
        ).reshape(micro_count, row_count, head_count, HD)
        value_heads = jnp.dot(flat_enc, layer[:, 2, :], preferred_element_type=jnp.float32).astype(
            jnp.bfloat16
        ).reshape(micro_count, row_count, head_count, HD)

        scores = (
            jnp.einsum("jmqhe,mkhe->mhjqk", query_heads, key_heads, preferred_element_type=jnp.float32)
            * scale
        )
        prob_grad = jnp.einsum(
            "jmqhe,mkhe->mhjqk", grad_heads, value_heads, preferred_element_type=jnp.float32
        )
        local_peak = jnp.max(scores, axis=-1)
        local_exp = jnp.exp(scores - local_peak[..., None])
        local_sum = jnp.sum(local_exp, axis=-1)
        local_delta = jnp.sum(local_exp * prob_grad, axis=-1)
        stats = jnp.stack([local_peak, local_sum, local_delta])
        all_stats = gather_axis(stats, "dp", n_dp)
        peaks = all_stats[:, 0]
        peak = jnp.max(peaks, axis=0)
        weight = jnp.exp(peaks - peak[None])
        total = jnp.sum(all_stats[:, 1] * weight, axis=0)
        row_delta = jnp.sum(all_stats[:, 2] * weight, axis=0) / total

        attend_prob = jnp.exp(scores - peak[..., None]) / total[..., None]
        prob_rounded = attend_prob.astype(jnp.bfloat16)
        score_grad = (attend_prob * (prob_grad - row_delta[..., None]) * scale).astype(jnp.bfloat16)

        context_part = jnp.einsum(
            "mhjqk,mkhe->jmqhe", prob_rounded, value_heads, preferred_element_type=jnp.float32
        ).reshape(n_dp, micro_count, row_count, feat_width)
        context = jnp.sum(lax.all_to_all(context_part, "dp", 0, 0, tiled=False), axis=0)
        context = context.astype(jnp.bfloat16)

        key_grad = jnp.einsum(
            "mhjqk,jmqhe->mkhe", score_grad, query_heads, preferred_element_type=jnp.float32
        ).astype(jnp.bfloat16)
        value_grad = jnp.einsum(
            "mhjqk,jmqhe->mkhe", prob_rounded, grad_heads, preferred_element_type=jnp.float32
        ).astype(jnp.bfloat16)
        head_terms = (
            jnp.einsum("rc,dc->rd", key_grad.reshape(rows, feat_width), layer[:, 1, :],
                       preferred_element_type=jnp.float32)
            + jnp.einsum("rc,dc->rd", value_grad.reshape(rows, feat_width), layer[:, 2, :],
                         preferred_element_type=jnp.float32)
        ).astype(jnp.bfloat16)
        head_terms = head_terms.reshape(micro_count, row_count, n_y, n_c, chunk_width)
        pair_sum = jnp.sum(
            lax.all_to_all(head_terms, "tc", 3, 0, tiled=False).astype(jnp.float32), axis=0
        ).astype(jnp.bfloat16)
        pair_sum = jnp.moveaxis(pair_sum, 2, 0)
        pair_sum = jnp.where(seg > 0, pair_sum, jnp.zeros_like(pair_sum))
        quarter = row_count // n_x
        pair_sum = pair_sum.reshape(n_y, micro_count, n_x, quarter, chunk_width)
        pair_sum = jnp.transpose(pair_sum, (2, 0, 1, 3, 4)).reshape(n_x * n_y, micro_count, quarter, chunk_width)
        heads_total = jnp.sum(
            lax.all_to_all(pair_sum, ("x", "ty"), 0, 0, tiled=False).astype(jnp.float32), axis=0
        )
        sections = seg_reduce(heads_total, n_hi, n_x)
        encoder_grad = (sections + upstream.astype(jnp.float32)).astype(jnp.bfloat16)
        return jnp.where(seg == 0, encoder_grad, context)

    outs = [
        chain(piece[m:m + 1], slots[:, :, m:m + 1], cotangent[0][m:m + 1])
        for m in range(micro_count)
    ]
    return jnp.concatenate(outs, axis=0)[None]


def solution(mesh):
    n_seg, n_dp, n_tensor = (mesh.shape[a] for a in ("segment", "dp", "tensor"))
    sub = Mesh(
        mesh.devices.reshape(n_seg // X_SIZE, X_SIZE, n_dp, n_tensor // 2, 2),
        SEG + ("dp",) + TEN,
    )
    placed = (
        P(SEG, None, "dp", None),
        P(SEG, None, None, TEN),
        P(SEG, None, "dp", TEN),
    )
    return jax.shard_map(
        shards,
        mesh=sub,
        in_specs=placed,
        out_specs=P(SEG, None, "dp", TEN),
        check_vma=False,
    )
```

```python
import jax
import jax.numpy as jnp
from jax import lax
from jax.sharding import Mesh, PartitionSpec as P

HD = 64
X_SIZE = 4
SEG = ("zh", "x")
TEN = ("ty", "tc")


def hi_rounds(n_hi):
    rounds = [[(0, 1)] + ([(0, n_hi - 1)] if n_hi > 2 else [])]
    if n_hi > 3:
        rounds.append([(1, 2)])
    return rounds


def gather_axis(value, axis, n):
    spread = jnp.broadcast_to(value[None], (n,) + value.shape)
    return lax.all_to_all(spread, axis, 0, 0, tiled=False)


def seg_broadcast(value, n_hi, n_x):
    x = lax.axis_index("x")
    zh = lax.axis_index("zh")
    quarter = value.shape[1] // n_x
    pieces = value.reshape(value.shape[0], n_x, quarter, value.shape[2])
    mine = pieces[:, 0]
    for k in range(1, n_x):
        got = lax.ppermute(pieces[:, k], "x", [(0, k)])
        mine = jnp.where(x == k, got, mine)
    out = mine
    for b in range(1, n_hi):
        got = lax.ppermute(mine, "zh", [(0, b)])
        out = jnp.where(zh == b, got, out)
    return out


def seg_reduce(mine, n_hi, n_x):
    zh = lax.axis_index("zh")
    sent = mine.astype(jnp.bfloat16)
    acc = mine
    for b in range(1, n_hi):
        got = lax.ppermute(sent, "zh", [(b, 0)])
        acc = acc + got.astype(jnp.float32)
    acc = jnp.where(zh == 0, acc, mine)
    parts = [acc]
    sent = acc.astype(jnp.bfloat16)
    for k in range(1, n_x):
        parts.append(lax.ppermute(sent, "x", [(k, 0)]).astype(jnp.float32))
    stacked = jnp.stack(parts, axis=1)
    return stacked.reshape(stacked.shape[0], -1, stacked.shape[-1])


def shards(inbound, weights, cotangent):
    n_hi = lax.axis_size("zh")
    n_x = lax.axis_size("x")
    n_dp = lax.axis_size("dp")
    n_y = lax.axis_size("ty")
    n_c = lax.axis_size("tc")
    n_tensor = n_y * n_c
    seg = lax.axis_index("zh") * n_x + lax.axis_index("x")
    core = lax.axis_index("tc")
    tix = lax.axis_index("ty") * n_c + core

    states = inbound[0]
    micro_count, row_count, model_width = states.shape
    layer = weights[0]
    feat_width = layer.shape[2]
    head_count = feat_width // HD
    scale = HD ** (-0.5)
    rows = micro_count * row_count
    chunk_width = model_width // n_tensor

    query = jnp.dot(
        states.reshape(rows, model_width), layer[:, 0, :], preferred_element_type=jnp.float32
    ).astype(jnp.bfloat16)
    query = query.reshape(micro_count, row_count, feat_width)
    slots = gather_axis(jnp.stack([query, cotangent[0]]), "dp", n_dp)

    chunk = lax.dynamic_slice_in_dim(states, tix * chunk_width, chunk_width, axis=2)
    piece = seg_broadcast(chunk, n_hi, n_x)
    slots, piece = lax.optimization_barrier((slots, piece))
    own = gather_axis(piece, ("x", "ty"), n_x * n_y)
    both = gather_axis(own, "tc", n_c)
    both = both.reshape(n_c, n_x, n_y, micro_count, row_count // n_x, chunk_width)
    query_heads = slots[:, 0].reshape(n_dp, micro_count, row_count, head_count, HD)
    grad_heads = slots[:, 1].reshape(n_dp, micro_count, row_count, head_count, HD)
    def project(kind):
        grid = layer[:, kind, :].reshape(n_y, n_c, chunk_width, feat_width)
        out = jnp.einsum("cxymrf,ycfn->mxrn", both, grid, preferred_element_type=jnp.float32)
        return out.astype(jnp.bfloat16).reshape(micro_count, row_count, head_count, HD)

    key_heads = project(1)
    value_heads = project(2)

    scores = (
        jnp.einsum("jmqhe,mkhe->mhjqk", query_heads, key_heads, preferred_element_type=jnp.float32)
        * scale
    )
    prob_grad = jnp.einsum(
        "jmqhe,mkhe->mhjqk", grad_heads, value_heads, preferred_element_type=jnp.float32
    )
    local_peak = jnp.max(scores, axis=-1)
    local_exp = jnp.exp(scores - local_peak[..., None])
    local_sum = jnp.sum(local_exp, axis=-1)
    local_delta = jnp.sum(local_exp * prob_grad, axis=-1)
    stats = jnp.stack([local_peak, local_sum, local_delta])
    all_stats = gather_axis(stats, "dp", n_dp)
    peaks = all_stats[:, 0]
    peak = jnp.max(peaks, axis=0)
    weight = jnp.exp(peaks - peak[None])
    total = jnp.sum(all_stats[:, 1] * weight, axis=0)
    row_delta = jnp.sum(all_stats[:, 2] * weight, axis=0) / total

    attend_prob = jnp.exp(scores - peak[..., None]) / total[..., None]
    prob_rounded = attend_prob.astype(jnp.bfloat16)
    score_grad = (attend_prob * (prob_grad - row_delta[..., None]) * scale).astype(jnp.bfloat16)

    context_part = jnp.einsum(
        "mhjqk,mkhe->jmqhe", prob_rounded, value_heads, preferred_element_type=jnp.float32
    ).reshape(n_dp, micro_count, row_count, feat_width)
    context = jnp.sum(lax.all_to_all(context_part, "dp", 0, 0, tiled=False), axis=0)
    context = context.astype(jnp.bfloat16)

    key_grad = jnp.einsum(
        "mhjqk,jmqhe->mkhe", score_grad, query_heads, preferred_element_type=jnp.float32
    ).astype(jnp.bfloat16)
    value_grad = jnp.einsum(
        "mhjqk,jmqhe->mkhe", prob_rounded, grad_heads, preferred_element_type=jnp.float32
    ).astype(jnp.bfloat16)
    def back(grad, kind):
        grid = layer[:, kind, :].reshape(n_y, n_c, chunk_width, feat_width)
        return jnp.einsum("mrn,ycfn->cmryf", grad.reshape(micro_count, row_count, feat_width), grid,
                          preferred_element_type=jnp.float32)

    head_terms = (back(key_grad, 1) + back(value_grad, 2)).astype(jnp.bfloat16)
    pair_sum = jnp.sum(
        lax.all_to_all(head_terms, "tc", 0, 0, tiled=False).astype(jnp.float32), axis=0
    ).astype(jnp.bfloat16)
    pair_sum = jnp.moveaxis(pair_sum, 2, 0)
    pair_sum = jnp.where(seg > 0, pair_sum, jnp.zeros_like(pair_sum))
    quarter = row_count // n_x
    pair_sum = pair_sum.reshape(n_y, micro_count, n_x, quarter, chunk_width)
    pair_sum = jnp.transpose(pair_sum, (2, 0, 1, 3, 4)).reshape(n_x * n_y, micro_count, quarter, chunk_width)
    heads_total = jnp.sum(
        lax.all_to_all(pair_sum, ("x", "ty"), 0, 0, tiled=False).astype(jnp.float32), axis=0
    )
    sections = seg_reduce(heads_total, n_hi, n_x)
    encoder_grad = (sections + cotangent[0].astype(jnp.float32)).astype(jnp.bfloat16)
    result = jnp.where(seg == 0, encoder_grad, context)
    return result[None]


def solution(mesh):
    n_seg, n_dp, n_tensor = (mesh.shape[a] for a in ("segment", "dp", "tensor"))
    sub = Mesh(
        mesh.devices.reshape(n_seg // X_SIZE, X_SIZE, n_dp, n_tensor // 2, 2),
        SEG + ("dp",) + TEN,
    )
    placed = (
        P(SEG, None, "dp", None),
        P(SEG, None, None, TEN),
        P(SEG, None, "dp", TEN),
    )
    return jax.shard_map(
        shards,
        mesh=sub,
        in_specs=placed,
        out_specs=P(SEG, None, "dp", TEN),
        check_vma=False,
    )
```

```python
import jax
import jax.numpy as jnp
from jax import lax
from jax.sharding import Mesh, PartitionSpec as P

HD = 64
X_SIZE = 4
SEG = ("zh", "x")
TEN = ("ty", "tc")


def hi_rounds(n_hi):
    rounds = [[(0, 1)] + ([(0, n_hi - 1)] if n_hi > 2 else [])]
    if n_hi > 3:
        rounds.append([(1, 2)])
    return rounds


def gather_axis(value, axis, n):
    spread = jnp.broadcast_to(value[None], (n,) + value.shape)
    return lax.all_to_all(spread, axis, 0, 0, tiled=False)


def seg_broadcast(value, n_hi, n_x, held):
    x = lax.axis_index("x")
    zh = lax.axis_index("zh")
    quarter = value.shape[1] // n_x
    pieces = value.reshape(value.shape[0], n_x, quarter, value.shape[2])
    mine = pieces[:, 0]
    for k in range(1, n_x):
        got = lax.ppermute(pieces[:, k], "x", [(0, k)])
        mine = jnp.where(x == k, got, mine)
    mine, held = lax.optimization_barrier((mine, held))
    out = mine
    for b in range(1, n_hi):
        got = lax.ppermute(mine, "zh", [(0, b)])
        out = jnp.where(zh == b, got, out)
    return out, held


def seg_reduce(mine, n_hi, n_x):
    zh = lax.axis_index("zh")
    sent = mine.astype(jnp.bfloat16)
    acc = mine
    for b in range(1, n_hi):
        got = lax.ppermute(sent, "zh", [(b, 0)])
        acc = acc + got.astype(jnp.float32)
    acc = jnp.where(zh == 0, acc, mine)
    parts = [acc]
    sent = acc.astype(jnp.bfloat16)
    for k in range(1, n_x):
        parts.append(lax.ppermute(sent, "x", [(k, 0)]).astype(jnp.float32))
    stacked = jnp.stack(parts, axis=1)
    return stacked.reshape(stacked.shape[0], -1, stacked.shape[-1])


def shards(inbound, weights, cotangent):
    n_hi = lax.axis_size("zh")
    n_x = lax.axis_size("x")
    n_dp = lax.axis_size("dp")
    n_y = lax.axis_size("ty")
    n_c = lax.axis_size("tc")
    n_tensor = n_y * n_c
    seg = lax.axis_index("zh") * n_x + lax.axis_index("x")
    core = lax.axis_index("tc")
    tix = lax.axis_index("ty") * n_c + core

    states = inbound[0]
    micro_count, row_count, model_width = states.shape
    layer = weights[0]
    feat_width = layer.shape[2]
    head_count = feat_width // HD
    scale = HD ** (-0.5)
    rows = micro_count * row_count
    chunk_width = model_width // n_tensor

    chunk = lax.dynamic_slice_in_dim(states, tix * chunk_width, chunk_width, axis=2)
    piece, held = seg_broadcast(chunk, n_hi, n_x, (states, layer[:, 0, :], cotangent[0]))
    held_states, query_weights, upstream = held
    query = jnp.dot(
        held_states.reshape(rows, model_width), query_weights, preferred_element_type=jnp.float32
    ).astype(jnp.bfloat16)
    query = query.reshape(micro_count, row_count, feat_width)
    slots = gather_axis(jnp.stack([query, upstream]), "dp", n_dp)
    own = gather_axis(piece, ("x", "ty"), n_x * n_y)
    both = gather_axis(own, "tc", n_c)
    both = both.reshape(n_c, n_x, n_y, micro_count, row_count // n_x, chunk_width)
    query_heads = slots[:, 0].reshape(n_dp, micro_count, row_count, head_count, HD)
    grad_heads = slots[:, 1].reshape(n_dp, micro_count, row_count, head_count, HD)
    def project(kind):
        grid = layer[:, kind, :].reshape(n_y, n_c, chunk_width, feat_width)
        out = jnp.einsum("cxymrf,ycfn->mxrn", both, grid, preferred_element_type=jnp.float32)
        return out.astype(jnp.bfloat16).reshape(micro_count, row_count, head_count, HD)

    key_heads = project(1)
    value_heads = project(2)

    scores = (
        jnp.einsum("jmqhe,mkhe->mhjqk", query_heads, key_heads, preferred_element_type=jnp.float32)
        * scale
    )
    prob_grad = jnp.einsum(
        "jmqhe,mkhe->mhjqk", grad_heads, value_heads, preferred_element_type=jnp.float32
    )
    local_peak = jnp.max(scores, axis=-1)
    local_exp = jnp.exp(scores - local_peak[..., None])
    local_sum = jnp.sum(local_exp, axis=-1)
    local_delta = jnp.sum(local_exp * prob_grad, axis=-1)
    stats = jnp.stack([local_peak, local_sum, local_delta])
    all_stats = gather_axis(stats, "dp", n_dp)
    peaks = all_stats[:, 0]
    peak = jnp.max(peaks, axis=0)
    weight = jnp.exp(peaks - peak[None])
    total = jnp.sum(all_stats[:, 1] * weight, axis=0)
    row_delta = jnp.sum(all_stats[:, 2] * weight, axis=0) / total

    attend_prob = jnp.exp(scores - peak[..., None]) / total[..., None]
    prob_rounded = attend_prob.astype(jnp.bfloat16)
    score_grad = (attend_prob * (prob_grad - row_delta[..., None]) * scale).astype(jnp.bfloat16)

    context_part = jnp.einsum(
        "mhjqk,mkhe->jmqhe", prob_rounded, value_heads, preferred_element_type=jnp.float32
    ).reshape(n_dp, micro_count, row_count, feat_width)
    context = jnp.sum(lax.all_to_all(context_part, "dp", 0, 0, tiled=False), axis=0)
    context = context.astype(jnp.bfloat16)

    key_grad = jnp.einsum(
        "mhjqk,jmqhe->mkhe", score_grad, query_heads, preferred_element_type=jnp.float32
    ).astype(jnp.bfloat16)
    value_grad = jnp.einsum(
        "mhjqk,jmqhe->mkhe", prob_rounded, grad_heads, preferred_element_type=jnp.float32
    ).astype(jnp.bfloat16)
    def back(grad, kind):
        grid = layer[:, kind, :].reshape(n_y, n_c, chunk_width, feat_width)
        return jnp.einsum("mrn,ycfn->cmryf", grad.reshape(micro_count, row_count, feat_width), grid,
                          preferred_element_type=jnp.float32)

    head_terms = (back(key_grad, 1) + back(value_grad, 2)).astype(jnp.bfloat16)
    pair_sum = jnp.sum(
        lax.all_to_all(head_terms, "tc", 0, 0, tiled=False).astype(jnp.float32), axis=0
    ).astype(jnp.bfloat16)
    pair_sum = jnp.moveaxis(pair_sum, 2, 0)
    pair_sum = jnp.where(seg > 0, pair_sum, jnp.zeros_like(pair_sum))
    quarter = row_count // n_x
    pair_sum = pair_sum.reshape(n_y, micro_count, n_x, quarter, chunk_width)
    pair_sum = jnp.transpose(pair_sum, (2, 0, 1, 3, 4)).reshape(n_x * n_y, micro_count, quarter, chunk_width)
    heads_total = jnp.sum(
        lax.all_to_all(pair_sum, ("x", "ty"), 0, 0, tiled=False).astype(jnp.float32), axis=0
    )
    sections = seg_reduce(heads_total, n_hi, n_x)
    encoder_grad = (sections + cotangent[0].astype(jnp.float32)).astype(jnp.bfloat16)
    result = jnp.where(seg == 0, encoder_grad, context)
    return result[None]


def solution(mesh):
    n_seg, n_dp, n_tensor = (mesh.shape[a] for a in ("segment", "dp", "tensor"))
    sub = Mesh(
        mesh.devices.reshape(n_seg // X_SIZE, X_SIZE, n_dp, n_tensor // 2, 2),
        SEG + ("dp",) + TEN,
    )
    placed = (
        P(SEG, None, "dp", None),
        P(SEG, None, None, TEN),
        P(SEG, None, "dp", TEN),
    )
    return jax.shard_map(
        shards,
        mesh=sub,
        in_specs=placed,
        out_specs=P(SEG, None, "dp", TEN),
        check_vma=False,
    )
```

```python
import jax
import jax.numpy as jnp
from jax import lax
from jax.sharding import Mesh, PartitionSpec as P

HD = 64
X_SIZE = 4
SEG = ("zh", "x")
TEN = ("ty", "tc")


def hi_rounds(n_hi):
    rounds = [[(0, 1)] + ([(0, n_hi - 1)] if n_hi > 2 else [])]
    if n_hi > 3:
        rounds.append([(1, 2)])
    return rounds


def gather_axis(value, axis, n):
    spread = jnp.broadcast_to(value[None], (n,) + value.shape)
    return lax.all_to_all(spread, axis, 0, 0, tiled=False)


def seg_broadcast(value, n_hi, n_x):
    zh = lax.axis_index("zh")
    quarter = value.shape[1] // n_x
    pieces = value.reshape(value.shape[0], n_x, quarter, value.shape[2])
    mine = lax.all_to_all(jnp.moveaxis(pieces, 1, 0), "x", 0, 0, tiled=False)[0]
    out = mine
    for b in range(1, n_hi):
        got = lax.ppermute(mine, "zh", [(0, b)])
        out = jnp.where(zh == b, got, out)
    return out


def seg_reduce(mine, n_hi, n_x):
    zh = lax.axis_index("zh")
    sent = mine.astype(jnp.bfloat16)
    acc = mine
    for b in range(1, n_hi):
        got = lax.ppermute(sent, "zh", [(b, 0)])
        acc = acc + got.astype(jnp.float32)
    acc = jnp.where(zh == 0, acc, mine)
    parts = gather_axis(acc.astype(jnp.bfloat16), "x", n_x).astype(jnp.float32)
    parts = jnp.where(jnp.arange(n_x)[:, None, None, None] == 0, acc[None], parts)
    stacked = jnp.moveaxis(parts, 0, 1)
    return stacked.reshape(stacked.shape[0], -1, stacked.shape[-1])


def shards(inbound, weights, cotangent):
    n_hi = lax.axis_size("zh")
    n_x = lax.axis_size("x")
    n_dp = lax.axis_size("dp")
    n_y = lax.axis_size("ty")
    n_c = lax.axis_size("tc")
    n_tensor = n_y * n_c
    seg = lax.axis_index("zh") * n_x + lax.axis_index("x")
    core = lax.axis_index("tc")
    tix = lax.axis_index("ty") * n_c + core

    states = inbound[0]
    micro_count, row_count, model_width = states.shape
    layer = weights[0]
    feat_width = layer.shape[2]
    head_count = feat_width // HD
    scale = HD ** (-0.5)
    rows = micro_count * row_count
    chunk_width = model_width // n_tensor

    query = jnp.dot(
        states.reshape(rows, model_width), layer[:, 0, :], preferred_element_type=jnp.float32
    ).astype(jnp.bfloat16)
    query = query.reshape(micro_count, row_count, feat_width)
    slots = gather_axis(jnp.stack([query, cotangent[0]]), "dp", n_dp)

    chunk = lax.dynamic_slice_in_dim(states, tix * chunk_width, chunk_width, axis=2)
    piece = seg_broadcast(chunk, n_hi, n_x)
    slots, piece = lax.optimization_barrier((slots, piece))
    own = gather_axis(piece, ("x", "ty"), n_x * n_y)
    both = gather_axis(own, "tc", n_c)
    both = both.reshape(n_c, n_x, n_y, micro_count, row_count // n_x, chunk_width)
    query_heads = slots[:, 0].reshape(n_dp, micro_count, row_count, head_count, HD)
    grad_heads = slots[:, 1].reshape(n_dp, micro_count, row_count, head_count, HD)
    def project(kind):
        grid = layer[:, kind, :].reshape(n_y, n_c, chunk_width, feat_width)
        out = jnp.einsum("cxymrf,ycfn->mxrn", both, grid, preferred_element_type=jnp.float32)
        return out.astype(jnp.bfloat16).reshape(micro_count, row_count, head_count, HD)

    key_heads = project(1)
    value_heads = project(2)

    scores = (
        jnp.einsum("jmqhe,mkhe->mhjqk", query_heads, key_heads, preferred_element_type=jnp.float32)
        * scale
    )
    prob_grad = jnp.einsum(
        "jmqhe,mkhe->mhjqk", grad_heads, value_heads, preferred_element_type=jnp.float32
    )
    local_peak = jnp.max(scores, axis=-1)
    local_exp = jnp.exp(scores - local_peak[..., None])
    local_sum = jnp.sum(local_exp, axis=-1)
    local_delta = jnp.sum(local_exp * prob_grad, axis=-1)
    stats = jnp.stack([local_peak, local_sum, local_delta])
    all_stats = gather_axis(stats, "dp", n_dp)
    peaks = all_stats[:, 0]
    peak = jnp.max(peaks, axis=0)
    weight = jnp.exp(peaks - peak[None])
    total = jnp.sum(all_stats[:, 1] * weight, axis=0)
    row_delta = jnp.sum(all_stats[:, 2] * weight, axis=0) / total

    attend_prob = jnp.exp(scores - peak[..., None]) / total[..., None]
    prob_rounded = attend_prob.astype(jnp.bfloat16)
    score_grad = (attend_prob * (prob_grad - row_delta[..., None]) * scale).astype(jnp.bfloat16)

    context_part = jnp.einsum(
        "mhjqk,mkhe->jmqhe", prob_rounded, value_heads, preferred_element_type=jnp.float32
    ).reshape(n_dp, micro_count, row_count, feat_width)
    context = jnp.sum(lax.all_to_all(context_part, "dp", 0, 0, tiled=False), axis=0)
    context = context.astype(jnp.bfloat16)

    key_grad = jnp.einsum(
        "mhjqk,jmqhe->mkhe", score_grad, query_heads, preferred_element_type=jnp.float32
    ).astype(jnp.bfloat16)
    value_grad = jnp.einsum(
        "mhjqk,jmqhe->mkhe", prob_rounded, grad_heads, preferred_element_type=jnp.float32
    ).astype(jnp.bfloat16)
    def back(grad, kind):
        grid = layer[:, kind, :].reshape(n_y, n_c, chunk_width, feat_width)
        return jnp.einsum("mrn,ycfn->cmryf", grad.reshape(micro_count, row_count, feat_width), grid,
                          preferred_element_type=jnp.float32)

    head_terms = (back(key_grad, 1) + back(value_grad, 2)).astype(jnp.bfloat16)
    pair_sum = jnp.sum(
        lax.all_to_all(head_terms, "tc", 0, 0, tiled=False).astype(jnp.float32), axis=0
    ).astype(jnp.bfloat16)
    pair_sum = jnp.moveaxis(pair_sum, 2, 0)
    pair_sum = jnp.where(seg > 0, pair_sum, jnp.zeros_like(pair_sum))
    quarter = row_count // n_x
    pair_sum = pair_sum.reshape(n_y, micro_count, n_x, quarter, chunk_width)
    pair_sum = jnp.transpose(pair_sum, (2, 0, 1, 3, 4)).reshape(n_x * n_y, micro_count, quarter, chunk_width)
    heads_total = jnp.sum(
        lax.all_to_all(pair_sum, ("x", "ty"), 0, 0, tiled=False).astype(jnp.float32), axis=0
    )
    sections = seg_reduce(heads_total, n_hi, n_x)
    encoder_grad = (sections + cotangent[0].astype(jnp.float32)).astype(jnp.bfloat16)
    result = jnp.where(seg == 0, encoder_grad, context)
    return result[None]


def solution(mesh):
    n_seg, n_dp, n_tensor = (mesh.shape[a] for a in ("segment", "dp", "tensor"))
    sub = Mesh(
        mesh.devices.reshape(n_seg // X_SIZE, X_SIZE, n_dp, n_tensor // 2, 2),
        SEG + ("dp",) + TEN,
    )
    placed = (
        P(SEG, None, "dp", None),
        P(SEG, None, None, TEN),
        P(SEG, None, "dp", TEN),
    )
    return jax.shard_map(
        shards,
        mesh=sub,
        in_specs=placed,
        out_specs=P(SEG, None, "dp", TEN),
        check_vma=False,
    )
```

```python
import jax
import jax.numpy as jnp
from jax import lax
from jax.sharding import Mesh, PartitionSpec as P

HD = 64
X_SIZE = 4
SEG = ("zh", "x")
TEN = ("ty", "tc")


def hi_rounds(n_hi):
    rounds = [[(0, 1)] + ([(0, n_hi - 1)] if n_hi > 2 else [])]
    if n_hi > 3:
        rounds.append([(1, 2)])
    return rounds


def gather_axis(value, axis, n):
    spread = jnp.broadcast_to(value[None], (n,) + value.shape)
    return lax.all_to_all(spread, axis, 0, 0, tiled=False)


def seg_broadcast(value, n_hi, n_x):
    x = lax.axis_index("x")
    zh = lax.axis_index("zh")
    quarter = value.shape[1] // n_x
    pieces = value.reshape(value.shape[0], n_x, quarter, value.shape[2])
    mine = pieces[:, 0]
    for k in range(1, n_x):
        got = lax.ppermute(pieces[:, k], "x", [(0, k)])
        mine = jnp.where(x == k, got, mine)
    out = mine
    for b in range(1, n_hi):
        got = lax.ppermute(mine, "zh", [(0, b)])
        out = jnp.where(zh == b, got, out)
    return out


def seg_reduce(mine, n_hi, n_x):
    zh = lax.axis_index("zh")
    sent = mine.astype(jnp.bfloat16)
    acc = mine
    for b in range(1, n_hi):
        got = lax.ppermute(sent, "zh", [(b, 0)])
        acc = acc + got.astype(jnp.float32)
    acc = jnp.where(zh == 0, acc, mine)
    parts = gather_axis(acc.astype(jnp.bfloat16), "x", n_x).astype(jnp.float32)
    parts = jnp.where(jnp.arange(n_x)[:, None, None, None] == 0, acc[None], parts)
    stacked = jnp.moveaxis(parts, 0, 1)
    return stacked.reshape(stacked.shape[0], -1, stacked.shape[-1])


def shards(inbound, weights, cotangent):
    n_hi = lax.axis_size("zh")
    n_x = lax.axis_size("x")
    n_dp = lax.axis_size("dp")
    n_y = lax.axis_size("ty")
    n_c = lax.axis_size("tc")
    n_tensor = n_y * n_c
    seg = lax.axis_index("zh") * n_x + lax.axis_index("x")
    core = lax.axis_index("tc")
    tix = lax.axis_index("ty") * n_c + core

    states = inbound[0]
    micro_count, row_count, model_width = states.shape
    layer = weights[0]
    feat_width = layer.shape[2]
    head_count = feat_width // HD
    scale = HD ** (-0.5)
    rows = micro_count * row_count
    chunk_width = model_width // n_tensor

    query = jnp.dot(
        states.reshape(rows, model_width), layer[:, 0, :], preferred_element_type=jnp.float32
    ).astype(jnp.bfloat16)
    query = query.reshape(micro_count, row_count, feat_width)
    slots = gather_axis(jnp.stack([query, cotangent[0]]), "dp", n_dp)

    chunk = lax.dynamic_slice_in_dim(states, tix * chunk_width, chunk_width, axis=2)
    piece = seg_broadcast(chunk, n_hi, n_x)
    slots, piece = lax.optimization_barrier((slots, piece))
    own = gather_axis(piece, ("x", "ty"), n_x * n_y)
    both = gather_axis(own, "tc", n_c)
    both = both.reshape(n_c, n_x, n_y, micro_count, row_count // n_x, chunk_width)
    query_heads = slots[:, 0].reshape(n_dp, micro_count, row_count, head_count, HD)
    grad_heads = slots[:, 1].reshape(n_dp, micro_count, row_count, head_count, HD)
    def project(kind):
        grid = layer[:, kind, :].reshape(n_y, n_c, chunk_width, feat_width)
        out = jnp.einsum("cxymrf,ycfn->mxrn", both, grid, preferred_element_type=jnp.float32)
        return out.astype(jnp.bfloat16).reshape(micro_count, row_count, head_count, HD)

    key_heads = project(1)
    value_heads = project(2)

    scores = (
        jnp.einsum("jmqhe,mkhe->mhjqk", query_heads, key_heads, preferred_element_type=jnp.float32)
        * scale
    )
    prob_grad = jnp.einsum(
        "jmqhe,mkhe->mhjqk", grad_heads, value_heads, preferred_element_type=jnp.float32
    )
    local_peak = jnp.max(scores, axis=-1)
    local_exp = jnp.exp(scores - local_peak[..., None])
    local_sum = jnp.sum(local_exp, axis=-1)
    local_delta = jnp.sum(local_exp * prob_grad, axis=-1)
    stats = jnp.stack([local_peak, local_sum, local_delta])
    all_stats = gather_axis(stats, "dp", n_dp)
    peaks = all_stats[:, 0]
    peak = jnp.max(peaks, axis=0)
    weight = jnp.exp(peaks - peak[None])
    total = jnp.sum(all_stats[:, 1] * weight, axis=0)
    row_delta = jnp.sum(all_stats[:, 2] * weight, axis=0) / total

    attend_prob = jnp.exp(scores - peak[..., None]) / total[..., None]
    prob_rounded = attend_prob.astype(jnp.bfloat16)
    score_grad = (attend_prob * (prob_grad - row_delta[..., None]) * scale).astype(jnp.bfloat16)

    context_part = jnp.einsum(
        "mhjqk,mkhe->jmqhe", prob_rounded, value_heads, preferred_element_type=jnp.float32
    ).reshape(n_dp, micro_count, row_count, feat_width)
    context = jnp.sum(lax.all_to_all(context_part, "dp", 0, 0, tiled=False), axis=0)
    context = context.astype(jnp.bfloat16)

    key_grad = jnp.einsum(
        "mhjqk,jmqhe->mkhe", score_grad, query_heads, preferred_element_type=jnp.float32
    ).astype(jnp.bfloat16)
    value_grad = jnp.einsum(
        "mhjqk,jmqhe->mkhe", prob_rounded, grad_heads, preferred_element_type=jnp.float32
    ).astype(jnp.bfloat16)
    def back(grad, kind):
        grid = layer[:, kind, :].reshape(n_y, n_c, chunk_width, feat_width)
        return jnp.einsum("mrn,ycfn->cmryf", grad.reshape(micro_count, row_count, feat_width), grid,
                          preferred_element_type=jnp.float32)

    head_terms = (back(key_grad, 1) + back(value_grad, 2)).astype(jnp.bfloat16)
    pair_sum = jnp.sum(
        lax.all_to_all(head_terms, "tc", 0, 0, tiled=False).astype(jnp.float32), axis=0
    ).astype(jnp.bfloat16)
    pair_sum = jnp.moveaxis(pair_sum, 2, 0)
    pair_sum = jnp.where(seg > 0, pair_sum, jnp.zeros_like(pair_sum))
    quarter = row_count // n_x
    pair_sum = pair_sum.reshape(n_y, micro_count, n_x, quarter, chunk_width)
    pair_sum = jnp.transpose(pair_sum, (2, 0, 1, 3, 4)).reshape(n_x * n_y, micro_count, quarter, chunk_width)
    heads_total = jnp.sum(
        lax.all_to_all(pair_sum, ("x", "ty"), 0, 0, tiled=False).astype(jnp.float32), axis=0
    )
    sections = seg_reduce(heads_total, n_hi, n_x)
    encoder_grad = (sections + cotangent[0].astype(jnp.float32)).astype(jnp.bfloat16)
    result = jnp.where(seg == 0, encoder_grad, context)
    return result[None]


def solution(mesh):
    n_seg, n_dp, n_tensor = (mesh.shape[a] for a in ("segment", "dp", "tensor"))
    sub = Mesh(
        mesh.devices.reshape(n_seg // X_SIZE, X_SIZE, n_dp, n_tensor // 2, 2),
        SEG + ("dp",) + TEN,
    )
    placed = (
        P(SEG, None, "dp", None),
        P(SEG, None, None, TEN),
        P(SEG, None, "dp", TEN),
    )
    return jax.shard_map(
        shards,
        mesh=sub,
        in_specs=placed,
        out_specs=P(SEG, None, "dp", TEN),
        check_vma=False,
    )
```
